256 devices in a mesh: row: 32 (over z, y), col: 8 (over x, core).
Axes of the slice: x: 4, y: 4, z: 8, core: 2. Of those that a mesh axis runs over, the one named last changes fastest.
Arguments:
- amps: bfloat16 [30720, 30720], P(('col', 'row')), may hold values from -6 to 6
- cycle_int: bfloat16 [30720, 1024], P('col'), may hold values from -0.03125 to 0.03125
- tile_mask: int32 [480, 16], P('col'), may hold values 0 or 1
- coulomb: bfloat16 [30720, 1024], P('row', 'col'), may hold values from -6 to 6
- occ_irrep: int32 [240], replicated, may hold values from 0 to 7
- vir_irrep: int32 [192], replicated, may hold values from 0 to 7
- occ_energy: float32 [240], replicated, may hold values from -1.5 to -0.3
- vir_energy: float32 [192], replicated, may hold values from 0.3 to 2
Outputs:
- new_amps: bfloat16 [30720, 1024], P('row', 'col')
The draws below stay inside these ranges and needn't reach their ends.
All inputs are finite; a program needn't handle non-finite values. No bound on the sum of `tile_mask` on one device may be relied on, other than what follows from the above.
Results may differ from the reference program's by a relative error of at most 0.001.
Values may be sent and summed in bfloat16 or wider, within the bound.
No kernel may reach another device: no remote copies, remote signals or barrier semaphores. Data moves between devices by JAX's collectives and lax.ppermute only.
A program may use at most 128 MiB of HBM per device.

```python
import jax
import jax.numpy as jnp
from jax import lax

O = 240
BLK = 64
KC = 30720
IA = 30720
JB = 1024
NAB = 2


def with_ends(array, rng, smallest, top_value):
    longest = array.shape.index(max(array.shape))
    spots = []
    for shift in (0, 1):
        where = [jax.random.randint(jax.random.fold_in(rng, axis), (), 0, length) for axis, length in enumerate(array.shape)]
        where[longest] = (where[longest] + shift) % array.shape[longest]
        spots.append(tuple(where))
    return array.at[spots[0]].set(smallest).at[spots[1]].set(top_value)


def block_levels(own_key, shape, shards, smallest, top_value):
    loudness, own = 1.0, jax.random.fold_in(own_key, 6)
    for position, blocks in shards:
        draws = jnp.exp(jax.random.uniform(jax.random.fold_in(own, position), (blocks,), jnp.float32, smallest / len(shards), top_value / len(shards)))
        loudness = loudness * jnp.repeat(draws, shape[position] // blocks).reshape([-1 if axis == position else 1 for axis in range(len(shape))])
    return loudness


def gaussian(key, shape, scale, limit, cuts=(), kind=jnp.bfloat16):
    array = scale * jax.random.normal(key, shape, jnp.float32)
    if cuts:
        array = array * block_levels(key, shape, cuts, -0.22, 0.18)
    return jnp.clip(array, -limit, limit).astype(kind)


def setup_inputs(seed: int = 0) -> dict:
    key_list = jax.random.split(jax.random.key(seed), 9)
    return {
        "amps": gaussian(key_list[0], (KC, IA), 1.0, 6.0, ((0, 256),)),
        "cycle_int": gaussian(key_list[1], (KC, JB), KC ** -0.5, 0.03125, ((0, 8),)),
        "tile_mask": with_ends((jax.random.randint(key_list[2], (KC // BLK, JB // BLK), 0, 4) < 3).astype(jnp.int32), jax.random.fold_in(key_list[2], 1), 0, 1),
        "coulomb": gaussian(key_list[3], (IA, JB), 1.0, 6.0, ((0, 32), (1, 8))),
        "occ_irrep": with_ends(jax.random.randint(key_list[4], (O,), 0, 8), jax.random.fold_in(key_list[4], 1), 0, 7).astype(jnp.int32),
        "vir_irrep": with_ends(jax.random.randint(key_list[5], ((NAB + 1) * BLK,), 0, 8), jax.random.fold_in(key_list[5], 1), 0, 7).astype(jnp.int32),
        "occ_energy": jnp.clip(jax.random.uniform(key_list[6], (O,), jnp.float32, -1.5, -0.3), -1.5, -0.3),
        "vir_energy": jnp.clip(jax.random.uniform(key_list[7], ((NAB + 1) * BLK,), jnp.float32, 0.3, 2.0), 0.3, 2.0),
    }


def reference(amps, cycle_int, tile_mask, coulomb, occ_irrep, vir_irrep, occ_energy, vir_energy):
    tiled_int = cycle_int.reshape(KC // BLK, BLK, JB // BLK, BLK)
    tile_keep = tile_mask.astype(jnp.bfloat16)[:, None, :, None]
    masked = (tiled_int * tile_keep).reshape(KC, JB)
    cycle_sum = lax.dot_general(amps, masked, (((0,), (0,)), ((), ())), preferred_element_type=jnp.float32)
    row_pos = jnp.arange(IA, dtype=jnp.int32)
    col_pos = jnp.arange(JB, dtype=jnp.int32)
    occ_row = (row_pos // BLK) % O
    vir_row = BLK * (row_pos // (O * BLK)) + row_pos % BLK
    occ_col = (col_pos // BLK) % O
    vir_col = col_pos % BLK + NAB * BLK
    sym_row = jnp.bitwise_xor(occ_irrep[occ_row], vir_irrep[vir_row])
    sym_col = jnp.bitwise_xor(occ_irrep[occ_col], vir_irrep[vir_col])
    allowed = sym_row[:, None] == sym_col[None, :]
    gap_row = vir_energy[vir_row] - occ_energy[occ_row]
    gap_col = vir_energy[vir_col] - occ_energy[occ_col]
    denominator = gap_row[:, None] + gap_col[None, :]
    updated = (coulomb.astype(jnp.float32) + cycle_sum) / denominator
    return jnp.where(allowed, updated, jnp.float32(0.0)).astype(jnp.bfloat16)
```

```python
import jax
import jax.numpy as jnp
from jax import lax
from jax.sharding import Mesh, PartitionSpec as P

BLK = 64

Z, Y, X, C = "z", "y", "x", "core"
COL = (X, C)
ROW = (Z, Y)


def lookup(positions, values_table):
    entries = jnp.arange(values_table.shape[0], dtype=jnp.int32)
    picked = jnp.where(
        positions[:, None] == entries[None, :],
        values_table[None, :],
        jnp.zeros((), values_table.dtype),
    )
    return jnp.sum(picked, axis=1)


def swap_perm(nz, nc):
    return [(z * nc + c, c * nz + z) for z in range(nz) for c in range(nc)]


def local(amps, cycle_int, tile_mask, coulomb, occ_irrep, vir_irrep, occ_energy, vir_energy):
    block_size = BLK
    occupied = occ_energy.shape[0]
    row_blocks = vir_energy.shape[0] // block_size - 1
    kc_rows, jb_all = cycle_int.shape
    rows_here, cols_here = coulomb.shape
    nz = lax.axis_size(Z)
    ny = lax.axis_size(Y)
    ncol = lax.axis_size(COL)
    z = lax.axis_index(Z)
    y = lax.axis_index(Y)
    c = lax.axis_index(COL)
    sub = amps.shape[0]
    span = sub * ny

    ci_rows = lax.dynamic_slice_in_dim(cycle_int, z * span, span, axis=0)
    mask_rows = jnp.repeat(tile_mask.astype(jnp.bfloat16), block_size, axis=0)
    mask_rows = lax.dynamic_slice_in_dim(mask_rows, z * span, span, axis=0)
    masked = (
        ci_rows.reshape(span, jb_all // block_size, block_size) * mask_rows[:, :, None]
    ).reshape(span, jb_all)
    masked_all = lax.all_gather(masked, COL, axis=0, tiled=True)

    plane_amps = lax.all_to_all(amps, (X, C, Y), split_axis=1, concat_axis=0, tiled=True)
    partial_value = lax.dot_general(
        plane_amps, masked_all, (((0,), (0,)), ((), ())), preferred_element_type=jnp.float32
    )
    cycle_sum = lax.psum_scatter(partial_value, Z, scatter_dimension=1, tiled=True)

    perm = swap_perm(nz, ncol)
    coulomb_here = lax.ppermute(coulomb, (Z, X, C), perm)
    row_block = c * ny + y
    row_pos = row_block * rows_here + jnp.arange(rows_here, dtype=jnp.int32)
    col_pos = z * cols_here + jnp.arange(cols_here, dtype=jnp.int32)
    occ_row = row_pos // block_size % occupied
    vir_row = block_size * (row_pos // (occupied * block_size)) + row_pos % block_size
    occ_col = col_pos // block_size % occupied
    vir_col = col_pos % block_size + row_blocks * block_size
    sym_row = jnp.bitwise_xor(lookup(occ_row, occ_irrep), lookup(vir_row, vir_irrep))
    sym_col = jnp.bitwise_xor(lookup(occ_col, occ_irrep), lookup(vir_col, vir_irrep))
    allowed = sym_row[:, None] == sym_col[None, :]
    gap_row = lookup(vir_row, vir_energy) - lookup(occ_row, occ_energy)
    gap_col = lookup(vir_col, vir_energy) - lookup(occ_col, occ_energy)
    denominator = gap_row[:, None] + gap_col[None, :]
    updated = (coulomb_here.astype(jnp.float32) + cycle_sum) / denominator
    out = jnp.where(allowed, updated, jnp.float32(0.0)).astype(jnp.bfloat16)
    return lax.ppermute(out, (Z, X, C), perm)


def solution(mesh):
    nrow, ncol = mesh.devices.shape
    ncore = 2
    nx = ncol // ncore
    nz = ncol
    ny = nrow // nz
    torus = Mesh(mesh.devices.reshape(nz, ny, nx, ncore), (Z, Y, X, C))
    return jax.shard_map(
        local,
        mesh=torus,
        in_specs=(
            P(COL + ROW, None),
            P(COL, None),
            P(COL, None),
            P(ROW, COL),
            P(),
            P(),
            P(),
            P(),
        ),
        out_specs=P(ROW, COL),
        check_vma=False,
    )
```

```python
import jax
import jax.numpy as jnp
from jax import lax
from jax.sharding import Mesh, PartitionSpec as P

BLK = 64
CHUNKS = 2

Z, Y, X, C = "z", "y", "x", "core"
COL = (X, C)
ROW = (Z, Y)


def lookup(positions, values_table):
    entries = jnp.arange(values_table.shape[0], dtype=jnp.int32)
    picked = jnp.where(
        positions[:, None] == entries[None, :],
        values_table[None, :],
        jnp.zeros((), values_table.dtype),
    )
    return jnp.sum(picked, axis=1)


def swap_perm(nz, nc):
    return [(z * nc + c, c * nz + z) for z in range(nz) for c in range(nc)]


def local(amps, cycle_int, tile_mask, coulomb, occ_irrep, vir_irrep, occ_energy, vir_energy):
    block_size = BLK
    occupied = occ_energy.shape[0]
    row_blocks = vir_energy.shape[0] // block_size - 1
    kc_rows, jb_all = cycle_int.shape
    rows_here, cols_here = coulomb.shape
    nz = lax.axis_size(Z)
    ny = lax.axis_size(Y)
    ncol = lax.axis_size(COL)
    z = lax.axis_index(Z)
    y = lax.axis_index(Y)
    c = lax.axis_index(COL)
    sub = amps.shape[0]
    span = sub * ny

    ci_rows = lax.dynamic_slice_in_dim(cycle_int, z * span, span, axis=0)
    mask_rows = jnp.repeat(tile_mask.astype(jnp.bfloat16), block_size, axis=0)
    mask_rows = lax.dynamic_slice_in_dim(mask_rows, z * span, span, axis=0)
    masked = (
        ci_rows.reshape(span, jb_all // block_size, block_size) * mask_rows[:, :, None]
    ).reshape(span, jb_all)
    masked_all = lax.all_gather(masked, COL, axis=0, tiled=True)

    groups = lax.axis_size((X, C, Y))
    width = amps.shape[1] // groups // CHUNKS
    pieces = amps.reshape(sub, groups, CHUNKS, width)
    sums = []
    previous = None
    for k in range(CHUNKS):
        piece = pieces[:, :, k, :].reshape(sub, groups * width)
        if previous is not None:
            previous, piece = lax.optimization_barrier((previous, piece))
            sums.append(lax.psum_scatter(previous, Z, scatter_dimension=1, tiled=True))
        plane_amps = lax.all_to_all(piece, (X, C, Y), split_axis=1, concat_axis=0, tiled=True)
        previous = lax.dot_general(
            plane_amps, masked_all, (((0,), (0,)), ((), ())), preferred_element_type=jnp.float32
        )
    sums.append(lax.psum_scatter(previous, Z, scatter_dimension=1, tiled=True))
    cycle_sum = jnp.concatenate(sums, axis=0)

    perm = swap_perm(nz, ncol)
    coulomb_here = lax.ppermute(coulomb, (Z, X, C), perm)
    row_block = c * ny + y
    row_pos = row_block * rows_here + jnp.arange(rows_here, dtype=jnp.int32)
    col_pos = z * cols_here + jnp.arange(cols_here, dtype=jnp.int32)
    occ_row = row_pos // block_size % occupied
    vir_row = block_size * (row_pos // (occupied * block_size)) + row_pos % block_size
    occ_col = col_pos // block_size % occupied
    vir_col = col_pos % block_size + row_blocks * block_size
    sym_row = jnp.bitwise_xor(lookup(occ_row, occ_irrep), lookup(vir_row, vir_irrep))
    sym_col = jnp.bitwise_xor(lookup(occ_col, occ_irrep), lookup(vir_col, vir_irrep))
    allowed = sym_row[:, None] == sym_col[None, :]
    gap_row = lookup(vir_row, vir_energy) - lookup(occ_row, occ_energy)
    gap_col = lookup(vir_col, vir_energy) - lookup(occ_col, occ_energy)
    denominator = gap_row[:, None] + gap_col[None, :]
    updated = (coulomb_here.astype(jnp.float32) + cycle_sum) / denominator
    out = jnp.where(allowed, updated, jnp.float32(0.0)).astype(jnp.bfloat16)
    return lax.ppermute(out, (Z, X, C), perm)


def solution(mesh):
    nrow, ncol = mesh.devices.shape
    ncore = 2
    nx = ncol // ncore
    nz = ncol
    ny = nrow // nz
    torus = Mesh(mesh.devices.reshape(nz, ny, nx, ncore), (Z, Y, X, C))
    return jax.shard_map(
        local,
        mesh=torus,
        in_specs=(
            P(COL + ROW, None),
            P(COL, None),
            P(COL, None),
            P(ROW, COL),
            P(),
            P(),
            P(),
            P(),
        ),
        out_specs=P(ROW, COL),
        check_vma=False,
    )
```

```python
import jax
import jax.numpy as jnp
from jax import lax
from jax.experimental import pallas as pl
from jax.experimental.pallas import tpu as pltpu
from jax.sharding import Mesh, PartitionSpec as P

BLK = 64

Z, Y, X, C = "z", "y", "x", "core"
COL = (X, C)
ROW = (Z, Y)


def lookup(positions, values_table):
    entries = jnp.arange(values_table.shape[0], dtype=jnp.int32)
    picked = jnp.where(
        positions[:, None] == entries[None, :],
        values_table[None, :],
        jnp.zeros((), values_table.dtype),
    )
    return jnp.sum(picked, axis=1)


def product_kernel(left_ref, right_ref, out_ref):
    out_ref[...] = jnp.dot(left_ref[...], right_ref[...], preferred_element_type=jnp.float32)


def product(left, right):
    rows, depth = left.shape
    width = right.shape[1]
    tile = 256
    return pl.pallas_call(
        product_kernel,
        out_shape=jax.ShapeDtypeStruct((rows, width), jnp.float32),
        grid=(rows // tile,),
        in_specs=[
            pl.BlockSpec((tile, depth), lambda i: (i, 0)),
            pl.BlockSpec((depth, width), lambda i: (0, 0)),
        ],
        out_specs=pl.BlockSpec((tile, width), lambda i: (i, 0)),
        cost_estimate=pl.CostEstimate(
            flops=2 * rows * depth * width,
            bytes_accessed=2 * rows * depth + 2 * depth * width + 4 * rows * width,
            transcendentals=0,
        ),
    )(left, right)


def chunk_widths(total):
    half = total // 2
    return [half, total - half]


def swap_perm(nz, nc):
    return [(z * nc + c, c * nz + z) for z in range(nz) for c in range(nc)]


def local(amps, cycle_int, tile_mask, coulomb, occ_irrep, vir_irrep, occ_energy, vir_energy):
    block_size = BLK
    occupied = occ_energy.shape[0]
    row_blocks = vir_energy.shape[0] // block_size - 1
    kc_rows, jb_all = cycle_int.shape
    rows_here, cols_here = coulomb.shape
    nz = lax.axis_size(Z)
    ny = lax.axis_size(Y)
    ncol = lax.axis_size(COL)
    z = lax.axis_index(Z)
    y = lax.axis_index(Y)
    c = lax.axis_index(COL)
    sub = amps.shape[0]
    span = sub * ny

    ci_rows = lax.dynamic_slice_in_dim(cycle_int, z * span, span, axis=0)
    mask_rows = jnp.repeat(tile_mask.astype(jnp.bfloat16), block_size, axis=0)
    mask_rows = lax.dynamic_slice_in_dim(mask_rows, z * span, span, axis=0)
    masked = (
        ci_rows.reshape(span, jb_all // block_size, block_size) * mask_rows[:, :, None]
    ).reshape(span, jb_all)
    masked_all_t = lax.all_gather(masked.T, COL, axis=1, tiled=True)

    groups = lax.axis_size((X, C, Y))
    pieces = amps.reshape(sub, groups, amps.shape[1] // groups)
    sums = []
    start = 0
    for width in chunk_widths(pieces.shape[2]):
        piece = jnp.transpose(pieces[:, :, start:start + width], (1, 0, 2))
        start += width
        plane_amps = lax.all_to_all(piece, (X, C, Y), split_axis=0, concat_axis=0, tiled=True)
        partial_value = product(masked_all_t, plane_amps.reshape(groups * sub, width))
        sums.append(lax.psum_scatter(partial_value, Z, scatter_dimension=0, tiled=True))
    cycle_sum = jnp.concatenate(sums, axis=1).T

    perm = swap_perm(nz, ncol)
    coulomb_here = lax.ppermute(coulomb, (Z, X, C), perm)
    row_block = c * ny + y
    row_pos = row_block * rows_here + jnp.arange(rows_here, dtype=jnp.int32)
    col_pos = z * cols_here + jnp.arange(cols_here, dtype=jnp.int32)
    occ_row = row_pos // block_size % occupied
    vir_row = block_size * (row_pos // (occupied * block_size)) + row_pos % block_size
    occ_col = col_pos // block_size % occupied
    vir_col = col_pos % block_size + row_blocks * block_size
    sym_row = jnp.bitwise_xor(lookup(occ_row, occ_irrep), lookup(vir_row, vir_irrep))
    sym_col = jnp.bitwise_xor(lookup(occ_col, occ_irrep), lookup(vir_col, vir_irrep))
    allowed = sym_row[:, None] == sym_col[None, :]
    gap_row = lookup(vir_row, vir_energy) - lookup(occ_row, occ_energy)
    gap_col = lookup(vir_col, vir_energy) - lookup(occ_col, occ_energy)
    denominator = gap_row[:, None] + gap_col[None, :]
    updated = (coulomb_here.astype(jnp.float32) + cycle_sum) / denominator
    out = jnp.where(allowed, updated, jnp.float32(0.0)).astype(jnp.bfloat16)
    return lax.ppermute(out, (Z, X, C), perm)


def solution(mesh):
    nrow, ncol = mesh.devices.shape
    ncore = 2
    nx = ncol // ncore
    nz = ncol
    ny = nrow // nz
    torus = Mesh(mesh.devices.reshape(nz, ny, nx, ncore), (Z, Y, X, C))
    return jax.shard_map(
        local,
        mesh=torus,
        in_specs=(
            P(COL + ROW, None),
            P(COL, None),
            P(COL, None),
            P(ROW, COL),
            P(),
            P(),
            P(),
            P(),
        ),
        out_specs=P(ROW, COL),
        check_vma=False,
    )
```

```python
import jax
import jax.numpy as jnp
from jax import lax
from jax.experimental import pallas as pl
from jax.experimental.pallas import tpu as pltpu
from jax.sharding import Mesh, PartitionSpec as P

BLK = 64

Z, Y, X, C = "z", "y", "x", "core"
COL = (X, C)
ROW = (Z, Y)


def lookup(positions, values_table):
    entries = jnp.arange(values_table.shape[0], dtype=jnp.int32)
    picked = jnp.where(
        positions[:, None] == entries[None, :],
        values_table[None, :],
        jnp.zeros((), values_table.dtype),
    )
    return jnp.sum(picked, axis=1)


def product_kernel(left_ref, right_ref, out_ref):
    out_ref[...] = lax.dot_general(
        left_ref[...], right_ref[...], (((0,), (0,)), ((), ())), preferred_element_type=jnp.float32
    )


def product(left, right):
    depth, rows = left.shape
    width = right.shape[1]
    tile = 256
    return pl.pallas_call(
        product_kernel,
        out_shape=jax.ShapeDtypeStruct((rows, width), jnp.float32),
        grid=(width // tile,),
        in_specs=[
            pl.BlockSpec((depth, rows), lambda j: (0, 0)),
            pl.BlockSpec((depth, tile), lambda j: (0, j)),
        ],
        out_specs=pl.BlockSpec((rows, tile), lambda j: (0, j)),
        cost_estimate=pl.CostEstimate(
            flops=2 * rows * depth * width,
            bytes_accessed=2 * rows * depth + 2 * depth * width + 4 * rows * width,
            transcendentals=0,
        ),
    )(left, right)


def chunk_widths(total):
    half = total // 2
    return [half, total - half]


def swap_perm(nz, nc):
    return [(z * nc + c, c * nz + z) for z in range(nz) for c in range(nc)]


def local(amps, cycle_int, tile_mask, coulomb, occ_irrep, vir_irrep, occ_energy, vir_energy):
    block_size = BLK
    occupied = occ_energy.shape[0]
    row_blocks = vir_energy.shape[0] // block_size - 1
    kc_rows, jb_all = cycle_int.shape
    rows_here, cols_here = coulomb.shape
    nz = lax.axis_size(Z)
    ny = lax.axis_size(Y)
    ncol = lax.axis_size(COL)
    z = lax.axis_index(Z)
    y = lax.axis_index(Y)
    c = lax.axis_index(COL)
    sub = amps.shape[0]
    span = sub * ny

    ci_rows = lax.dynamic_slice_in_dim(cycle_int, z * span, span, axis=0)
    mask_rows = jnp.repeat(tile_mask.astype(jnp.bfloat16), block_size, axis=0)
    mask_rows = lax.dynamic_slice_in_dim(mask_rows, z * span, span, axis=0)
    masked = (
        ci_rows.reshape(span, jb_all // block_size, block_size) * mask_rows[:, :, None]
    ).reshape(span, jb_all)
    masked_all = lax.all_gather(masked, COL, axis=0, tiled=True)

    groups = lax.axis_size((X, C, Y))
    block = amps.shape[1] // groups
    sums = []
    start = 0
    for width in chunk_widths(block):
        piece = jnp.stack(
            [amps[:, g * block + start:g * block + start + width] for g in range(groups)]
        )
        start += width
        plane_amps = lax.all_to_all(piece, (X, C, Y), split_axis=0, concat_axis=0, tiled=True)
        partial_value = product(plane_amps.reshape(groups * sub, width), masked_all)
        sums.append(lax.psum_scatter(partial_value, Z, scatter_dimension=1, tiled=True))
    cycle_sum = jnp.concatenate(sums, axis=0)

    perm = swap_perm(nz, ncol)
    coulomb_here = lax.ppermute(coulomb, (Z, X, C), perm)
    row_block = c * ny + y
    row_pos = row_block * rows_here + jnp.arange(rows_here, dtype=jnp.int32)
    col_pos = z * cols_here + jnp.arange(cols_here, dtype=jnp.int32)
    occ_row = row_pos // block_size % occupied
    vir_row = block_size * (row_pos // (occupied * block_size)) + row_pos % block_size
    occ_col = col_pos // block_size % occupied
    vir_col = col_pos % block_size + row_blocks * block_size
    sym_row = jnp.bitwise_xor(lookup(occ_row, occ_irrep), lookup(vir_row, vir_irrep))
    sym_col = jnp.bitwise_xor(lookup(occ_col, occ_irrep), lookup(vir_col, vir_irrep))
    allowed = sym_row[:, None] == sym_col[None, :]
    gap_row = lookup(vir_row, vir_energy) - lookup(occ_row, occ_energy)
    gap_col = lookup(vir_col, vir_energy) - lookup(occ_col, occ_energy)
    denominator = gap_row[:, None] + gap_col[None, :]
    updated = (coulomb_here.astype(jnp.float32) + cycle_sum) / denominator
    out = jnp.where(allowed, updated, jnp.float32(0.0)).astype(jnp.bfloat16)
    return lax.ppermute(out, (Z, X, C), perm)


def solution(mesh):
    nrow, ncol = mesh.devices.shape
    ncore = 2
    nx = ncol // ncore
    nz = ncol
    ny = nrow // nz
    torus = Mesh(mesh.devices.reshape(nz, ny, nx, ncore), (Z, Y, X, C))
    return jax.shard_map(
        local,
        mesh=torus,
        in_specs=(
            P(COL + ROW, None),
            P(COL, None),
            P(COL, None),
            P(ROW, COL),
            P(),
            P(),
            P(),
            P(),
        ),
        out_specs=P(ROW, COL),
        check_vma=False,
    )
```

```python
import functools

import jax
import jax.numpy as jnp
from jax import lax
from jax.experimental import pallas as pl
from jax.experimental.pallas import tpu as pltpu
from jax.sharding import Mesh, PartitionSpec as P

BLK = 64

Z, Y, X, C = "z", "y", "x", "core"
COL = (X, C)
ROW = (Z, Y)


def lookup(positions, values_table):
    entries = jnp.arange(values_table.shape[0], dtype=jnp.int32)
    picked = jnp.where(
        positions[:, None] == entries[None, :],
        values_table[None, :],
        jnp.zeros((), values_table.dtype),
    )
    return jnp.sum(picked, axis=1)


def product_kernel(left_ref, right_ref, out_ref):
    out_ref[...] = lax.dot_general(
        left_ref[...], right_ref[...], (((0,), (0,)), ((), ())), preferred_element_type=jnp.float32
    )


def product(left, right):
    depth, rows = left.shape
    width = right.shape[1]
    tile = 256
    return pl.pallas_call(
        product_kernel,
        out_shape=jax.ShapeDtypeStruct((rows, width), jnp.float32),
        grid=(width // tile,),
        in_specs=[
            pl.BlockSpec((depth, rows), lambda j: (0, 0)),
            pl.BlockSpec((depth, tile), lambda j: (0, j)),
        ],
        out_specs=pl.BlockSpec((rows, tile), lambda j: (0, j)),
        cost_estimate=pl.CostEstimate(
            flops=2 * rows * depth * width,
            bytes_accessed=2 * rows * depth + 2 * depth * width + 4 * rows * width,
            transcendentals=0,
        ),
    )(left, right)


def stack_kernel(widths, block, in_ref, *out_refs):
    for half in range(2):
        start = half * block
        for width, out_ref in zip(widths, out_refs):
            out_ref[half] = in_ref[:, start:start + width]
            start += width


def stack_chunks(amps, groups, widths):
    sub, total = amps.shape
    block = total // groups
    return pl.pallas_call(
        functools.partial(stack_kernel, widths, block),
        out_shape=[jax.ShapeDtypeStruct((groups, sub, width), amps.dtype) for width in widths],
        grid=(groups // 2,),
        in_specs=[pl.BlockSpec((sub, 2 * block), lambda h: (0, h))],
        out_specs=[pl.BlockSpec((2, sub, width), lambda h: (h, 0, 0)) for width in widths],
    )(amps)


def chunk_widths(total):
    half = total // 2
    return [half, total - half]


def swap_perm(nz, nc):
    return [(z * nc + c, c * nz + z) for z in range(nz) for c in range(nc)]


def local(amps, cycle_int, tile_mask, coulomb, occ_irrep, vir_irrep, occ_energy, vir_energy):
    block_size = BLK
    occupied = occ_energy.shape[0]
    row_blocks = vir_energy.shape[0] // block_size - 1
    kc_rows, jb_all = cycle_int.shape
    rows_here, cols_here = coulomb.shape
    nz = lax.axis_size(Z)
    ny = lax.axis_size(Y)
    ncol = lax.axis_size(COL)
    z = lax.axis_index(Z)
    y = lax.axis_index(Y)
    c = lax.axis_index(COL)
    sub = amps.shape[0]
    span = sub * ny

    ci_rows = lax.dynamic_slice_in_dim(cycle_int, z * span, span, axis=0)
    mask_rows = jnp.repeat(tile_mask.astype(jnp.bfloat16), block_size, axis=0)
    mask_rows = lax.dynamic_slice_in_dim(mask_rows, z * span, span, axis=0)
    masked = (
        ci_rows.reshape(span, jb_all // block_size, block_size) * mask_rows[:, :, None]
    ).reshape(span, jb_all)
    masked_all = lax.all_gather(masked, COL, axis=0, tiled=True)

    groups = lax.axis_size((X, C, Y))
    block = amps.shape[1] // groups
    widths = chunk_widths(block)
    sums = []
    for piece, width in zip(stack_chunks(amps, groups, widths), widths):
        plane_amps = lax.all_to_all(piece, (X, C, Y), split_axis=0, concat_axis=0, tiled=True)
        partial_value = product(plane_amps.reshape(groups * sub, width), masked_all)
        sums.append(lax.psum_scatter(partial_value, Z, scatter_dimension=1, tiled=True))
    cycle_sum = jnp.concatenate(sums, axis=0)

    perm = swap_perm(nz, ncol)
    coulomb_here = lax.ppermute(coulomb, (Z, X, C), perm)
    row_block = c * ny + y
    row_pos = row_block * rows_here + jnp.arange(rows_here, dtype=jnp.int32)
    col_pos = z * cols_here + jnp.arange(cols_here, dtype=jnp.int32)
    occ_row = row_pos // block_size % occupied
    vir_row = block_size * (row_pos // (occupied * block_size)) + row_pos % block_size
    occ_col = col_pos // block_size % occupied
    vir_col = col_pos % block_size + row_blocks * block_size
    sym_row = jnp.bitwise_xor(lookup(occ_row, occ_irrep), lookup(vir_row, vir_irrep))
    sym_col = jnp.bitwise_xor(lookup(occ_col, occ_irrep), lookup(vir_col, vir_irrep))
    allowed = sym_row[:, None] == sym_col[None, :]
    gap_row = lookup(vir_row, vir_energy) - lookup(occ_row, occ_energy)
    gap_col = lookup(vir_col, vir_energy) - lookup(occ_col, occ_energy)
    denominator = gap_row[:, None] + gap_col[None, :]
    updated = (coulomb_here.astype(jnp.float32) + cycle_sum) / denominator
    out = jnp.where(allowed, updated, jnp.float32(0.0)).astype(jnp.bfloat16)
    return lax.ppermute(out, (Z, X, C), perm)


def solution(mesh):
    nrow, ncol = mesh.devices.shape
    ncore = 2
    nx = ncol // ncore
    nz = ncol
    ny = nrow // nz
    torus = Mesh(mesh.devices.reshape(nz, ny, nx, ncore), (Z, Y, X, C))
    return jax.shard_map(
        local,
        mesh=torus,
        in_specs=(
            P(COL + ROW, None),
            P(COL, None),
            P(COL, None),
            P(ROW, COL),
            P(),
            P(),
            P(),
            P(),
        ),
        out_specs=P(ROW, COL),
        check_vma=False,
    )
```

```python
import functools

import jax
import jax.numpy as jnp
from jax import lax
from jax.experimental import pallas as pl
from jax.experimental.pallas import tpu as pltpu
from jax.sharding import Mesh, PartitionSpec as P

BLK = 64

Z, Y, X, C = "z", "y", "x", "core"
COL = (X, C)
ROW = (Z, Y)


def lookup(positions, values_table):
    entries = jnp.arange(values_table.shape[0], dtype=jnp.int32)
    picked = jnp.where(
        positions[:, None] == entries[None, :],
        values_table[None, :],
        jnp.zeros((), values_table.dtype),
    )
    return jnp.sum(picked, axis=1)


def product_kernel(left_ref, right_ref, out_ref):
    out_ref[...] = lax.dot_general(
        left_ref[...], right_ref[...], (((0,), (0,)), ((), ())), preferred_element_type=jnp.float32
    )


def product(left, right):
    depth, rows = left.shape
    width = right.shape[1]
    tile = 256
    return pl.pallas_call(
        product_kernel,
        out_shape=jax.ShapeDtypeStruct((rows, width), jnp.float32),
        grid=(width // tile,),
        in_specs=[
            pl.BlockSpec((depth, rows), lambda j: (0, 0)),
            pl.BlockSpec((depth, tile), lambda j: (0, j)),
        ],
        out_specs=pl.BlockSpec((rows, tile), lambda j: (0, j)),
        cost_estimate=pl.CostEstimate(
            flops=2 * rows * depth * width,
            bytes_accessed=2 * rows * depth + 2 * depth * width + 4 * rows * width,
            transcendentals=0,
        ),
    )(left, right)


def stack_kernel(widths, block, in_ref, *out_refs):
    for half in range(2):
        start = half * block
        for width, out_ref in zip(widths, out_refs):
            out_ref[half] = in_ref[:, start:start + width]
            start += width


def stack_chunks(amps, groups, widths):
    sub, total = amps.shape
    block = total // groups
    return pl.pallas_call(
        functools.partial(stack_kernel, widths, block),
        out_shape=[jax.ShapeDtypeStruct((groups, sub, width), amps.dtype) for width in widths],
        grid=(groups // 2,),
        in_specs=[pl.BlockSpec((sub, 2 * block), lambda h: (0, h))],
        out_specs=[pl.BlockSpec((2, sub, width), lambda h: (h, 0, 0)) for width in widths],
    )(amps)


def chunk_widths(total):
    half = total // 2
    return [half, total - half]


def owner_perm(nz, nx, ncore, to_owner):
    pairs = []
    for z in range(nz):
        for x in range(nx):
            for core in range(ncore):
                row_major = core * nx + x
                src = z * nx * ncore + x * ncore + core
                dst = row_major * nx * ncore + (z // ncore) * ncore + z % ncore
                pairs.append((src, dst) if to_owner else (dst, src))
    return pairs


def local(amps, cycle_int, tile_mask, coulomb, occ_irrep, vir_irrep, occ_energy, vir_energy):
    block_size = BLK
    occupied = occ_energy.shape[0]
    row_blocks = vir_energy.shape[0] // block_size - 1
    kc_rows, jb_all = cycle_int.shape
    rows_here, cols_here = coulomb.shape
    nz = lax.axis_size(Z)
    ny = lax.axis_size(Y)
    ncol = lax.axis_size(COL)
    z = lax.axis_index(Z)
    y = lax.axis_index(Y)
    c = lax.axis_index(COL)
    sub = amps.shape[0]
    span = sub * ny

    ci_rows = lax.dynamic_slice_in_dim(cycle_int, z * span, span, axis=0)
    mask_rows = jnp.repeat(tile_mask.astype(jnp.bfloat16), block_size, axis=0)
    mask_rows = lax.dynamic_slice_in_dim(mask_rows, z * span, span, axis=0)
    masked = (
        ci_rows.reshape(span, jb_all // block_size, block_size) * mask_rows[:, :, None]
    ).reshape(span, jb_all)
    masked_all = lax.all_gather(masked, X, axis=0, tiled=True)
    masked_all = lax.all_gather(masked_all, C, axis=0, tiled=True)

    groups = lax.axis_size((C, X, Y))
    block = amps.shape[1] // groups
    widths = chunk_widths(block)
    sums = []
    for piece, width in zip(stack_chunks(amps, groups, widths), widths):
        plane_amps = lax.all_to_all(piece, (C, X, Y), split_axis=0, concat_axis=0, tiled=True)
        partial_value = product(plane_amps.reshape(groups * sub, width), masked_all)
        sums.append(lax.psum_scatter(partial_value, Z, scatter_dimension=1, tiled=True))
    cycle_sum = jnp.concatenate(sums, axis=0)

    nx = lax.axis_size(X)
    ncore = lax.axis_size(C)
    coulomb_here = lax.ppermute(coulomb, (Z, X, C), owner_perm(nz, nx, ncore, False))
    row_block = (lax.axis_index(C) * nx + lax.axis_index(X)) * ny + y
    row_pos = row_block * rows_here + jnp.arange(rows_here, dtype=jnp.int32)
    col_pos = z * cols_here + jnp.arange(cols_here, dtype=jnp.int32)
    occ_row = row_pos // block_size % occupied
    vir_row = block_size * (row_pos // (occupied * block_size)) + row_pos % block_size
    occ_col = col_pos // block_size % occupied
    vir_col = col_pos % block_size + row_blocks * block_size
    sym_row = jnp.bitwise_xor(lookup(occ_row, occ_irrep), lookup(vir_row, vir_irrep))
    sym_col = jnp.bitwise_xor(lookup(occ_col, occ_irrep), lookup(vir_col, vir_irrep))
    allowed = sym_row[:, None] == sym_col[None, :]
    gap_row = lookup(vir_row, vir_energy) - lookup(occ_row, occ_energy)
    gap_col = lookup(vir_col, vir_energy) - lookup(occ_col, occ_energy)
    denominator = gap_row[:, None] + gap_col[None, :]
    updated = (coulomb_here.astype(jnp.float32) + cycle_sum) / denominator
    out = jnp.where(allowed, updated, jnp.float32(0.0)).astype(jnp.bfloat16)
    return lax.ppermute(out, (Z, X, C), owner_perm(nz, nx, ncore, True))


def solution(mesh):
    nrow, ncol = mesh.devices.shape
    ncore = 2
    nx = ncol // ncore
    nz = ncol
    ny = nrow // nz
    torus = Mesh(mesh.devices.reshape(nz, ny, nx, ncore), (Z, Y, X, C))
    return jax.shard_map(
        local,
        mesh=torus,
        in_specs=(
            P(COL + ROW, None),
            P(COL, None),
            P(COL, None),
            P(ROW, COL),
            P(),
            P(),
            P(),
            P(),
        ),
        out_specs=P(ROW, COL),
        check_vma=False,
    )
```

```python
import functools

import jax
import jax.numpy as jnp
from jax import lax
from jax.experimental import pallas as pl
from jax.experimental.pallas import tpu as pltpu
from jax.sharding import Mesh, PartitionSpec as P

BLK = 64

Z, Y, X, C = "z", "y", "x", "core"
COL = (X, C)
ROW = (Z, Y)


def lookup(positions, values_table):
    entries = jnp.arange(values_table.shape[0], dtype=jnp.int32)
    picked = jnp.where(
        positions[:, None] == entries[None, :],
        values_table[None, :],
        jnp.zeros((), values_table.dtype),
    )
    return jnp.sum(picked, axis=1)


def product_kernel(left_ref, right_ref, out_ref):
    out_ref[...] = lax.dot_general(
        left_ref[...], right_ref[...], (((0,), (0,)), ((), ())), preferred_element_type=jnp.float32
    )


def product(left, right):
    depth, rows = left.shape
    width = right.shape[1]
    tile = 256
    return pl.pallas_call(
        product_kernel,
        out_shape=jax.ShapeDtypeStruct((rows, width), jnp.float32),
        grid=(width // tile,),
        in_specs=[
            pl.BlockSpec((depth, rows), lambda j: (0, 0)),
            pl.BlockSpec((depth, tile), lambda j: (0, j)),
        ],
        out_specs=pl.BlockSpec((rows, tile), lambda j: (0, j)),
        cost_estimate=pl.CostEstimate(
            flops=2 * rows * depth * width,
            bytes_accessed=2 * rows * depth + 2 * depth * width + 4 * rows * width,
            transcendentals=0,
        ),
    )(left, right)


def stack_kernel(start, width, block, in_ref, out_ref):
    for half in range(2):
        out_ref[half] = in_ref[:, half * block + start:half * block + start + width]


def stack_chunk(amps, groups, start, width):
    sub, total = amps.shape
    block = total // groups
    return pl.pallas_call(
        functools.partial(stack_kernel, start, width, block),
        out_shape=jax.ShapeDtypeStruct((groups, sub, width), amps.dtype),
        grid=(groups // 2,),
        in_specs=[pl.BlockSpec((sub, 2 * block), lambda h: (0, h))],
        out_specs=pl.BlockSpec((2, sub, width), lambda h: (h, 0, 0)),
    )(amps)


def chunk_widths(total):
    first = total * 5 // 8
    return [first, total - first]


def swap_perm(nz, nc):
    return [(z * nc + c, c * nz + z) for z in range(nz) for c in range(nc)]


def local(amps, cycle_int, tile_mask, coulomb, occ_irrep, vir_irrep, occ_energy, vir_energy):
    block_size = BLK
    occupied = occ_energy.shape[0]
    row_blocks = vir_energy.shape[0] // block_size - 1
    kc_rows, jb_all = cycle_int.shape
    rows_here, cols_here = coulomb.shape
    nz = lax.axis_size(Z)
    ny = lax.axis_size(Y)
    ncol = lax.axis_size(COL)
    z = lax.axis_index(Z)
    y = lax.axis_index(Y)
    c = lax.axis_index(COL)
    sub = amps.shape[0]
    span = sub * ny

    ci_rows = lax.dynamic_slice_in_dim(cycle_int, z * span, span, axis=0)
    mask_rows = jnp.repeat(tile_mask.astype(jnp.bfloat16), block_size, axis=0)
    mask_rows = lax.dynamic_slice_in_dim(mask_rows, z * span, span, axis=0)
    masked = (
        ci_rows.reshape(span, jb_all // block_size, block_size) * mask_rows[:, :, None]
    ).reshape(span, jb_all)
    masked_all = lax.all_gather(masked, COL, axis=0, tiled=True)

    groups = lax.axis_size((X, C, Y))
    block = amps.shape[1] // groups
    sums = []
    start = 0
    for width in chunk_widths(block):
        piece = stack_chunk(amps, groups, start, width)
        start += width
        plane_amps = lax.all_to_all(piece, (X, C, Y), split_axis=0, concat_axis=0, tiled=True)
        partial_value = product(plane_amps.reshape(groups * sub, width), masked_all)
        sums.append(lax.psum_scatter(partial_value, Z, scatter_dimension=1, tiled=True))
    cycle_sum = jnp.concatenate(sums, axis=0)

    perm = swap_perm(nz, ncol)
    coulomb_here = lax.ppermute(coulomb, (Z, X, C), perm)
    row_block = c * ny + y
    row_pos = row_block * rows_here + jnp.arange(rows_here, dtype=jnp.int32)
    col_pos = z * cols_here + jnp.arange(cols_here, dtype=jnp.int32)
    occ_row = row_pos // block_size % occupied
    vir_row = block_size * (row_pos // (occupied * block_size)) + row_pos % block_size
    occ_col = col_pos // block_size % occupied
    vir_col = col_pos % block_size + row_blocks * block_size
    sym_row = jnp.bitwise_xor(lookup(occ_row, occ_irrep), lookup(vir_row, vir_irrep))
    sym_col = jnp.bitwise_xor(lookup(occ_col, occ_irrep), lookup(vir_col, vir_irrep))
    allowed = sym_row[:, None] == sym_col[None, :]
    gap_row = lookup(vir_row, vir_energy) - lookup(occ_row, occ_energy)
    gap_col = lookup(vir_col, vir_energy) - lookup(occ_col, occ_energy)
    denominator = gap_row[:, None] + gap_col[None, :]
    updated = (coulomb_here.astype(jnp.float32) + cycle_sum) / denominator
    out = jnp.where(allowed, updated, jnp.float32(0.0)).astype(jnp.bfloat16)
    return lax.ppermute(out, (Z, X, C), perm)


def solution(mesh):
    nrow, ncol = mesh.devices.shape
    ncore = 2
    nx = ncol // ncore
    nz = ncol
    ny = nrow // nz
    torus = Mesh(mesh.devices.reshape(nz, ny, nx, ncore), (Z, Y, X, C))
    return jax.shard_map(
        local,
        mesh=torus,
        in_specs=(
            P(COL + ROW, None),
            P(COL, None),
            P(COL, None),
            P(ROW, COL),
            P(),
            P(),
            P(),
            P(),
        ),
        out_specs=P(ROW, COL),
        check_vma=False,
    )
```

```python
import functools

import jax
import jax.numpy as jnp
from jax import lax
from jax.experimental import pallas as pl
from jax.experimental.pallas import tpu as pltpu
from jax.sharding import Mesh, PartitionSpec as P

BLK = 64

Z, Y, X, C = "z", "y", "x", "core"
COL = (X, C)
ROW = (Z, Y)


def lookup(positions, values_table):
    entries = jnp.arange(values_table.shape[0], dtype=jnp.int32)
    picked = jnp.where(
        positions[:, None] == entries[None, :],
        values_table[None, :],
        jnp.zeros((), values_table.dtype),
    )
    return jnp.sum(picked, axis=1)


def product_kernel(left_ref, right_ref, out_ref):
    out_ref[...] = lax.dot_general(
        left_ref[...], right_ref[...], (((0,), (0,)), ((), ())), preferred_element_type=jnp.float32
    )


def product(left, right):
    depth, rows = left.shape
    width = right.shape[1]
    tile = 256
    return pl.pallas_call(
        product_kernel,
        out_shape=jax.ShapeDtypeStruct((rows, width), jnp.float32),
        grid=(width // tile,),
        in_specs=[
            pl.BlockSpec((depth, rows), lambda j: (0, 0)),
            pl.BlockSpec((depth, tile), lambda j: (0, j)),
        ],
        out_specs=pl.BlockSpec((rows, tile), lambda j: (0, j)),
        cost_estimate=pl.CostEstimate(
            flops=2 * rows * depth * width,
            bytes_accessed=2 * rows * depth + 2 * depth * width + 4 * rows * width,
            transcendentals=0,
        ),
    )(left, right)


def stack_kernel(start, width, block, in_ref, out_ref):
    for half in range(2):
        out_ref[half] = in_ref[:, half * block + start:half * block + start + width]


def stack_chunk(amps, groups, start, width):
    sub, total = amps.shape
    block = total // groups
    return pl.pallas_call(
        functools.partial(stack_kernel, start, width, block),
        out_shape=jax.ShapeDtypeStruct((groups, sub, width), amps.dtype),
        grid=(groups // 2,),
        in_specs=[pl.BlockSpec((sub, 2 * block), lambda h: (0, h))],
        out_specs=pl.BlockSpec((2, sub, width), lambda h: (h, 0, 0)),
    )(amps)


def chunk_widths(total):
    first = total * 5 // 8
    return [first, total - first]


def swap_perm(nz, nc):
    return [(z * nc + c, c * nz + z) for z in range(nz) for c in range(nc)]


def local(amps, cycle_int, tile_mask, coulomb, occ_irrep, vir_irrep, occ_energy, vir_energy):
    block_size = BLK
    occupied = occ_energy.shape[0]
    row_blocks = vir_energy.shape[0] // block_size - 1
    kc_rows, jb_all = cycle_int.shape
    rows_here, cols_here = coulomb.shape
    nz = lax.axis_size(Z)
    ny = lax.axis_size(Y)
    ncol = lax.axis_size(COL)
    z = lax.axis_index(Z)
    y = lax.axis_index(Y)
    c = lax.axis_index(COL)
    sub = amps.shape[0]
    span = sub * ny

    ci_rows = lax.dynamic_slice_in_dim(cycle_int, z * span, span, axis=0)
    mask_rows = jnp.repeat(tile_mask.astype(jnp.bfloat16), block_size, axis=0)
    mask_rows = lax.dynamic_slice_in_dim(mask_rows, z * span, span, axis=0)
    masked = (
        ci_rows.reshape(span, jb_all // block_size, block_size) * mask_rows[:, :, None]
    ).reshape(span, jb_all)
    masked_all = lax.all_gather(masked, COL, axis=0, tiled=True)

    groups = lax.axis_size((X, C, Y))
    block = amps.shape[1] // groups
    perm = swap_perm(nz, ncol)
    coulomb_here = lax.ppermute(coulomb, (Z, X, C), perm)
    sums = []
    start = 0
    for k, width in enumerate(chunk_widths(block)):
        piece = stack_chunk(amps, groups, start, width)
        start += width
        if k == 1:
            coulomb_here, piece = lax.optimization_barrier((coulomb_here, piece))
        plane_amps = lax.all_to_all(piece, (X, C, Y), split_axis=0, concat_axis=0, tiled=True)
        partial_value = product(plane_amps.reshape(groups * sub, width), masked_all)
        sums.append(lax.psum_scatter(partial_value, Z, scatter_dimension=1, tiled=True))
    cycle_sum = jnp.concatenate(sums, axis=0)

    row_block = c * ny + y
    row_pos = row_block * rows_here + jnp.arange(rows_here, dtype=jnp.int32)
    col_pos = z * cols_here + jnp.arange(cols_here, dtype=jnp.int32)
    occ_row = row_pos // block_size % occupied
    vir_row = block_size * (row_pos // (occupied * block_size)) + row_pos % block_size
    occ_col = col_pos // block_size % occupied
    vir_col = col_pos % block_size + row_blocks * block_size
    sym_row = jnp.bitwise_xor(lookup(occ_row, occ_irrep), lookup(vir_row, vir_irrep))
    sym_col = jnp.bitwise_xor(lookup(occ_col, occ_irrep), lookup(vir_col, vir_irrep))
    allowed = sym_row[:, None] == sym_col[None, :]
    gap_row = lookup(vir_row, vir_energy) - lookup(occ_row, occ_energy)
    gap_col = lookup(vir_col, vir_energy) - lookup(occ_col, occ_energy)
    denominator = gap_row[:, None] + gap_col[None, :]
    updated = (coulomb_here.astype(jnp.float32) + cycle_sum) / denominator
    out = jnp.where(allowed, updated, jnp.float32(0.0)).astype(jnp.bfloat16)
    return lax.ppermute(out, (Z, X, C), perm)


def solution(mesh):
    nrow, ncol = mesh.devices.shape
    ncore = 2
    nx = ncol // ncore
    nz = ncol
    ny = nrow // nz
    torus = Mesh(mesh.devices.reshape(nz, ny, nx, ncore), (Z, Y, X, C))
    return jax.shard_map(
        local,
        mesh=torus,
        in_specs=(
            P(COL + ROW, None),
            P(COL, None),
            P(COL, None),
            P(ROW, COL),
            P(),
            P(),
            P(),
            P(),
        ),
        out_specs=P(ROW, COL),
        check_vma=False,
    )
```

```python
import functools

import jax
import jax.numpy as jnp
from jax import lax
from jax.experimental import pallas as pl
from jax.experimental.pallas import tpu as pltpu
from jax.sharding import Mesh, PartitionSpec as P

BLK = 64

Z, Y, X, C = "z", "y", "x", "core"
COL = (X, C)
ROW = (Z, Y)


def lookup(positions, values_table):
    entries = jnp.arange(values_table.shape[0], dtype=jnp.int32)
    picked = jnp.where(
        positions[:, None] == entries[None, :],
        values_table[None, :],
        jnp.zeros((), values_table.dtype),
    )
    return jnp.sum(picked, axis=1)


def product_kernel(left_ref, right_ref, out_ref):
    out_ref[...] = lax.dot_general(
        left_ref[...], right_ref[...], (((0,), (0,)), ((), ())), preferred_element_type=jnp.float32
    )


def product(left, right):
    depth, rows = left.shape
    width = right.shape[1]
    tile = 256
    return pl.pallas_call(
        product_kernel,
        out_shape=jax.ShapeDtypeStruct((rows, width), jnp.float32),
        grid=(width // tile,),
        in_specs=[
            pl.BlockSpec((depth, rows), lambda j: (0, 0)),
            pl.BlockSpec((depth, tile), lambda j: (0, j)),
        ],
        out_specs=pl.BlockSpec((rows, tile), lambda j: (0, j)),
        cost_estimate=pl.CostEstimate(
            flops=2 * rows * depth * width,
            bytes_accessed=2 * rows * depth + 2 * depth * width + 4 * rows * width,
            transcendentals=0,
        ),
    )(left, right)


def stack_kernel(start, width, block, in_ref, out_ref):
    for half in range(2):
        out_ref[half] = in_ref[:, half * block + start:half * block + start + width]


def stack_chunk(amps, groups, start, width):
    sub, total = amps.shape
    block = total // groups
    return pl.pallas_call(
        functools.partial(stack_kernel, start, width, block),
        out_shape=jax.ShapeDtypeStruct((groups, sub, width), amps.dtype),
        grid=(groups // 2,),
        in_specs=[pl.BlockSpec((sub, 2 * block), lambda h: (0, h))],
        out_specs=pl.BlockSpec((2, sub, width), lambda h: (h, 0, 0)),
    )(amps)


def chunk_widths(total):
    first = total * 5 // 8
    return [first, total - first]


def swap_perm(nz, nc):
    return [(z * nc + c, c * nz + z) for z in range(nz) for c in range(nc)]


def gather_cols(piece):
    nx = lax.axis_size(X)
    x = lax.axis_index(X)
    first = lax.axis_index(C) == 0
    swap = [(0, 1), (1, 0)]
    forward = [(i * 2, (i + 1) % nx * 2) for i in range(nx)]
    backward = [(i * 2 + 1, (i - 1) % nx * 2 + 1) for i in range(nx)]
    other = lax.ppermute(piece, C, swap)
    chip = jnp.where(first, jnp.concatenate([piece, other]), jnp.concatenate([other, piece]))
    near = lax.ppermute(chip, (X, C), forward + backward)
    near_other = lax.ppermute(near, C, swap)
    half = chip.shape[1] // 2
    ahead = lax.ppermute(
        jnp.where(first, near[:, :half], near[:, half:]), (X, C), forward + backward
    )
    ahead_other = lax.ppermute(ahead, C, swap)
    far = jnp.where(
        first,
        jnp.concatenate([ahead, ahead_other], axis=1),
        jnp.concatenate([ahead_other, ahead], axis=1),
    )
    following = jnp.where(first, near_other, near)
    preceding = jnp.where(first, near, near_other)
    chips = jnp.stack([chip, following, far, preceding])
    chips = jnp.take(chips, (jnp.arange(nx) - x) % nx, axis=0)
    return chips.reshape(nx * chip.shape[0], chip.shape[1])


def local(amps, cycle_int, tile_mask, coulomb, occ_irrep, vir_irrep, occ_energy, vir_energy):
    block_size = BLK
    occupied = occ_energy.shape[0]
    row_blocks = vir_energy.shape[0] // block_size - 1
    kc_rows, jb_all = cycle_int.shape
    rows_here, cols_here = coulomb.shape
    nz = lax.axis_size(Z)
    ny = lax.axis_size(Y)
    ncol = lax.axis_size(COL)
    z = lax.axis_index(Z)
    y = lax.axis_index(Y)
    c = lax.axis_index(COL)
    sub = amps.shape[0]
    span = sub * ny

    ci_rows = lax.dynamic_slice_in_dim(cycle_int, z * span, span, axis=0)
    mask_rows = jnp.repeat(tile_mask.astype(jnp.bfloat16), block_size, axis=0)
    mask_rows = lax.dynamic_slice_in_dim(mask_rows, z * span, span, axis=0)
    masked = (
        ci_rows.reshape(span, jb_all // block_size, block_size) * mask_rows[:, :, None]
    ).reshape(span, jb_all)
    masked_all = gather_cols(masked)

    groups = lax.axis_size((X, C, Y))
    block = amps.shape[1] // groups
    perm = swap_perm(nz, ncol)
    coulomb_here = lax.ppermute(coulomb, (Z, X, C), perm)
    sums = []
    start = 0
    for k, width in enumerate(chunk_widths(block)):
        piece = stack_chunk(amps, groups, start, width)
        start += width
        if k == 1:
            coulomb_here, piece = lax.optimization_barrier((coulomb_here, piece))
        plane_amps = lax.all_to_all(piece, (X, C, Y), split_axis=0, concat_axis=0, tiled=True)
        partial_value = product(plane_amps.reshape(groups * sub, width), masked_all)
        sums.append(lax.psum_scatter(partial_value, Z, scatter_dimension=1, tiled=True))
    cycle_sum = jnp.concatenate(sums, axis=0)

    row_block = c * ny + y
    row_pos = row_block * rows_here + jnp.arange(rows_here, dtype=jnp.int32)
    col_pos = z * cols_here + jnp.arange(cols_here, dtype=jnp.int32)
    occ_row = row_pos // block_size % occupied
    vir_row = block_size * (row_pos // (occupied * block_size)) + row_pos % block_size
    occ_col = col_pos // block_size % occupied
    vir_col = col_pos % block_size + row_blocks * block_size
    sym_row = jnp.bitwise_xor(lookup(occ_row, occ_irrep), lookup(vir_row, vir_irrep))
    sym_col = jnp.bitwise_xor(lookup(occ_col, occ_irrep), lookup(vir_col, vir_irrep))
    allowed = sym_row[:, None] == sym_col[None, :]
    gap_row = lookup(vir_row, vir_energy) - lookup(occ_row, occ_energy)
    gap_col = lookup(vir_col, vir_energy) - lookup(occ_col, occ_energy)
    denominator = gap_row[:, None] + gap_col[None, :]
    updated = (coulomb_here.astype(jnp.float32) + cycle_sum) / denominator
    out = jnp.where(allowed, updated, jnp.float32(0.0)).astype(jnp.bfloat16)
    return lax.ppermute(out, (Z, X, C), perm)


def solution(mesh):
    nrow, ncol = mesh.devices.shape
    ncore = 2
    nx = ncol // ncore
    nz = ncol
    ny = nrow // nz
    torus = Mesh(mesh.devices.reshape(nz, ny, nx, ncore), (Z, Y, X, C))
    return jax.shard_map(
        local,
        mesh=torus,
        in_specs=(
            P(COL + ROW, None),
            P(COL, None),
            P(COL, None),
            P(ROW, COL),
            P(),
            P(),
            P(),
            P(),
        ),
        out_specs=P(ROW, COL),
        check_vma=False,
    )
```

```python
import functools

import jax
import jax.numpy as jnp
from jax import lax
from jax.experimental import pallas as pl
from jax.experimental.pallas import tpu as pltpu
from jax.sharding import Mesh, PartitionSpec as P

BLK = 64

Z, Y, X, C = "z", "y", "x", "core"
COL = (X, C)
ROW = (Z, Y)


def lookup(positions, values_table):
    entries = jnp.arange(values_table.shape[0], dtype=jnp.int32)
    picked = jnp.where(
        positions[:, None] == entries[None, :],
        values_table[None, :],
        jnp.zeros((), values_table.dtype),
    )
    return jnp.sum(picked, axis=1)


def product_kernel(left_ref, right_ref, out_ref):
    out_ref[...] = lax.dot_general(
        left_ref[...], right_ref[...], (((0,), (0,)), ((), ())), preferred_element_type=jnp.float32
    )


def product(left, right):
    depth, rows = left.shape
    width = right.shape[1]
    tile = 256
    return pl.pallas_call(
        product_kernel,
        out_shape=jax.ShapeDtypeStruct((rows, width), jnp.float32),
        grid=(width // tile,),
        in_specs=[
            pl.BlockSpec((depth, rows), lambda j: (0, 0)),
            pl.BlockSpec((depth, tile), lambda j: (0, j)),
        ],
        out_specs=pl.BlockSpec((rows, tile), lambda j: (0, j)),
        cost_estimate=pl.CostEstimate(
            flops=2 * rows * depth * width,
            bytes_accessed=2 * rows * depth + 2 * depth * width + 4 * rows * width,
            transcendentals=0,
        ),
    )(left, right)


def stack_kernel(start, width, block, in_ref, out_ref):
    for half in range(2):
        out_ref[half] = in_ref[:, half * block + start:half * block + start + width]


def stack_chunk(amps, groups, start, width):
    sub, total = amps.shape
    block = total // groups
    return pl.pallas_call(
        functools.partial(stack_kernel, start, width, block),
        out_shape=jax.ShapeDtypeStruct((groups, sub, width), amps.dtype),
        grid=(groups // 2,),
        in_specs=[pl.BlockSpec((sub, 2 * block), lambda h: (0, h))],
        out_specs=pl.BlockSpec((2, sub, width), lambda h: (h, 0, 0)),
    )(amps)


def chunk_widths(total):
    last = total * 4 // 15
    return [total - last, last]


def swap_perm(nz, nc):
    return [(z * nc + c, c * nz + z) for z in range(nz) for c in range(nc)]


def local(amps, cycle_int, tile_mask, coulomb, occ_irrep, vir_irrep, occ_energy, vir_energy):
    block_size = BLK
    occupied = occ_energy.shape[0]
    row_blocks = vir_energy.shape[0] // block_size - 1
    kc_rows, jb_all = cycle_int.shape
    rows_here, cols_here = coulomb.shape
    nz = lax.axis_size(Z)
    ny = lax.axis_size(Y)
    ncol = lax.axis_size(COL)
    z = lax.axis_index(Z)
    y = lax.axis_index(Y)
    c = lax.axis_index(COL)
    sub = amps.shape[0]
    span = sub * ny

    ci_rows = lax.dynamic_slice_in_dim(cycle_int, z * span, span, axis=0)
    mask_rows = jnp.repeat(tile_mask.astype(jnp.bfloat16), block_size, axis=0)
    mask_rows = lax.dynamic_slice_in_dim(mask_rows, z * span, span, axis=0)
    masked = (
        ci_rows.reshape(span, jb_all // block_size, block_size) * mask_rows[:, :, None]
    ).reshape(span, jb_all)
    masked_all = lax.all_gather(masked, COL, axis=0, tiled=True)

    groups = lax.axis_size((X, C, Y))
    block = amps.shape[1] // groups
    perm = swap_perm(nz, ncol)
    coulomb_here = lax.ppermute(coulomb, (Z, X, C), perm)
    sums = []
    start = 0
    for k, width in enumerate(chunk_widths(block)):
        piece = stack_chunk(amps, groups, start, width)
        start += width
        if k == 1:
            coulomb_here, piece = lax.optimization_barrier((coulomb_here, piece))
        plane_amps = lax.all_to_all(piece, (X, C, Y), split_axis=0, concat_axis=0, tiled=True)
        partial_value = product(plane_amps.reshape(groups * sub, width), masked_all)
        sums.append(lax.psum_scatter(partial_value, Z, scatter_dimension=1, tiled=True))
    cycle_sum = jnp.concatenate(sums, axis=0)

    row_block = c * ny + y
    row_pos = row_block * rows_here + jnp.arange(rows_here, dtype=jnp.int32)
    col_pos = z * cols_here + jnp.arange(cols_here, dtype=jnp.int32)
    occ_row = row_pos // block_size % occupied
    vir_row = block_size * (row_pos // (occupied * block_size)) + row_pos % block_size
    occ_col = col_pos // block_size % occupied
    vir_col = col_pos % block_size + row_blocks * block_size
    sym_row = jnp.bitwise_xor(lookup(occ_row, occ_irrep), lookup(vir_row, vir_irrep))
    sym_col = jnp.bitwise_xor(lookup(occ_col, occ_irrep), lookup(vir_col, vir_irrep))
    allowed = sym_row[:, None] == sym_col[None, :]
    gap_row = lookup(vir_row, vir_energy) - lookup(occ_row, occ_energy)
    gap_col = lookup(vir_col, vir_energy) - lookup(occ_col, occ_energy)
    denominator = gap_row[:, None] + gap_col[None, :]
    updated = (coulomb_here.astype(jnp.float32) + cycle_sum) / denominator
    out = jnp.where(allowed, updated, jnp.float32(0.0)).astype(jnp.bfloat16)
    return lax.ppermute(out, (Z, X, C), perm)


def solution(mesh):
    nrow, ncol = mesh.devices.shape
    ncore = 2
    nx = ncol // ncore
    nz = ncol
    ny = nrow // nz
    torus = Mesh(mesh.devices.reshape(nz, ny, nx, ncore), (Z, Y, X, C))
    return jax.shard_map(
        local,
        mesh=torus,
        in_specs=(
            P(COL + ROW, None),
            P(COL, None),
            P(COL, None),
            P(ROW, COL),
            P(),
            P(),
            P(),
            P(),
        ),
        out_specs=P(ROW, COL),
        check_vma=False,
    )
```

```python
import functools

import jax
import jax.numpy as jnp
from jax import lax
from jax.experimental import pallas as pl
from jax.experimental.pallas import tpu as pltpu
from jax.sharding import Mesh, PartitionSpec as P

BLK = 64

Z, Y, X, C = "z", "y", "x", "core"
COL = (X, C)
ROW = (Z, Y)


def lookup(positions, values_table):
    entries = jnp.arange(values_table.shape[0], dtype=jnp.int32)
    picked = jnp.where(
        positions[:, None] == entries[None, :],
        values_table[None, :],
        jnp.zeros((), values_table.dtype),
    )
    return jnp.sum(picked, axis=1)


def product_kernel(left_ref, right_ref, out_ref):
    out_ref[...] = lax.dot_general(
        left_ref[...], right_ref[...], (((0,), (0,)), ((), ())), preferred_element_type=jnp.float32
    )


def product(left, right):
    depth, rows = left.shape
    width = right.shape[1]
    tile = 256
    return pl.pallas_call(
        product_kernel,
        out_shape=jax.ShapeDtypeStruct((rows, width), jnp.float32),
        grid=(width // tile,),
        in_specs=[
            pl.BlockSpec((depth, rows), lambda j: (0, 0)),
            pl.BlockSpec((depth, tile), lambda j: (0, j)),
        ],
        out_specs=pl.BlockSpec((rows, tile), lambda j: (0, j)),
        cost_estimate=pl.CostEstimate(
            flops=2 * rows * depth * width,
            bytes_accessed=2 * rows * depth + 2 * depth * width + 4 * rows * width,
            transcendentals=0,
        ),
    )(left, right)


def stack_kernel(start, width, block, in_ref, out_ref):
    for half in range(2):
        out_ref[half] = in_ref[:, half * block + start:half * block + start + width]


def stack_chunk(amps, groups, start, width):
    sub, total = amps.shape
    block = total // groups
    return pl.pallas_call(
        functools.partial(stack_kernel, start, width, block),
        out_shape=jax.ShapeDtypeStruct((groups, sub, width), amps.dtype),
        grid=(groups // 2,),
        in_specs=[pl.BlockSpec((sub, 2 * block), lambda h: (0, h))],
        out_specs=pl.BlockSpec((2, sub, width), lambda h: (h, 0, 0)),
    )(amps)


def chunk_widths(total):
    first = total * 5 // 8
    return [first, total - first]


def swap_perm(nz, nc):
    return [(z * nc + c, c * nz + z) for z in range(nz) for c in range(nc)]


def local(amps, cycle_int, tile_mask, coulomb, occ_irrep, vir_irrep, occ_energy, vir_energy):
    block_size = BLK
    occupied = occ_energy.shape[0]
    row_blocks = vir_energy.shape[0] // block_size - 1
    kc_rows, jb_all = cycle_int.shape
    rows_here, cols_here = coulomb.shape
    nz = lax.axis_size(Z)
    ny = lax.axis_size(Y)
    ncol = lax.axis_size(COL)
    z = lax.axis_index(Z)
    y = lax.axis_index(Y)
    c = lax.axis_index(COL)
    sub = amps.shape[0]
    span = sub * ny

    ci_rows = lax.dynamic_slice_in_dim(cycle_int, z * span, span, axis=0)
    mask_rows = jnp.repeat(tile_mask.astype(jnp.bfloat16), block_size, axis=0)
    mask_rows = lax.dynamic_slice_in_dim(mask_rows, z * span, span, axis=0)
    masked = (
        ci_rows.reshape(span, jb_all // block_size, block_size) * mask_rows[:, :, None]
    ).reshape(span, jb_all)
    masked_all = lax.all_gather(masked, COL, axis=0, tiled=True)

    groups = lax.axis_size((X, C, Y))
    block = amps.shape[1] // groups
    perm = swap_perm(nz, ncol)
    coulomb_here = lax.ppermute(coulomb, (Z, X, C), perm)
    sums = []
    start = 0
    for k, width in enumerate(chunk_widths(block)):
        piece = stack_chunk(amps, groups, start, width)
        start += width
        if k == 1:
            coulomb_here, piece, partial_value = lax.optimization_barrier(
                (coulomb_here, piece, partial_value)
            )
            sums[-1] = lax.psum_scatter(partial_value, Z, scatter_dimension=1, tiled=True)
        plane_amps = lax.all_to_all(piece, (X, C, Y), split_axis=0, concat_axis=0, tiled=True)
        partial_value = product(plane_amps.reshape(groups * sub, width), masked_all)
        sums.append(lax.psum_scatter(partial_value, Z, scatter_dimension=1, tiled=True))
    cycle_sum = jnp.concatenate(sums, axis=0)

    row_block = c * ny + y
    row_pos = row_block * rows_here + jnp.arange(rows_here, dtype=jnp.int32)
    col_pos = z * cols_here + jnp.arange(cols_here, dtype=jnp.int32)
    occ_row = row_pos // block_size % occupied
    vir_row = block_size * (row_pos // (occupied * block_size)) + row_pos % block_size
    occ_col = col_pos // block_size % occupied
    vir_col = col_pos % block_size + row_blocks * block_size
    sym_row = jnp.bitwise_xor(lookup(occ_row, occ_irrep), lookup(vir_row, vir_irrep))
    sym_col = jnp.bitwise_xor(lookup(occ_col, occ_irrep), lookup(vir_col, vir_irrep))
    allowed = sym_row[:, None] == sym_col[None, :]
    gap_row = lookup(vir_row, vir_energy) - lookup(occ_row, occ_energy)
    gap_col = lookup(vir_col, vir_energy) - lookup(occ_col, occ_energy)
    denominator = gap_row[:, None] + gap_col[None, :]
    updated = (coulomb_here.astype(jnp.float32) + cycle_sum) / denominator
    out = jnp.where(allowed, updated, jnp.float32(0.0)).astype(jnp.bfloat16)
    return lax.ppermute(out, (Z, X, C), perm)


def solution(mesh):
    nrow, ncol = mesh.devices.shape
    ncore = 2
    nx = ncol // ncore
    nz = ncol
    ny = nrow // nz
    torus = Mesh(mesh.devices.reshape(nz, ny, nx, ncore), (Z, Y, X, C))
    return jax.shard_map(
        local,
        mesh=torus,
        in_specs=(
            P(COL + ROW, None),
            P(COL, None),
            P(COL, None),
            P(ROW, COL),
            P(),
            P(),
            P(),
            P(),
        ),
        out_specs=P(ROW, COL),
        check_vma=False,
    )
```

```python
import functools

import jax
import jax.numpy as jnp
from jax import lax
from jax.experimental import pallas as pl
from jax.experimental.pallas import tpu as pltpu
from jax.sharding import Mesh, PartitionSpec as P

BLK = 64

Z, Y, X, C = "z", "y", "x", "core"
COL = (X, C)
ROW = (Z, Y)


def lookup(positions, values_table):
    entries = jnp.arange(values_table.shape[0], dtype=jnp.int32)
    picked = jnp.where(
        positions[:, None] == entries[None, :],
        values_table[None, :],
        jnp.zeros((), values_table.dtype),
    )
    return jnp.sum(picked, axis=1)


def product_kernel(left_ref, right_ref, out_ref):
    out_ref[...] = lax.dot_general(
        left_ref[...], right_ref[...], (((0,), (0,)), ((), ())), preferred_element_type=jnp.float32
    )


def product(left, right):
    depth, rows = left.shape
    width = right.shape[1]
    tile = 256
    return pl.pallas_call(
        product_kernel,
        out_shape=jax.ShapeDtypeStruct((rows, width), jnp.float32),
        grid=(width // tile,),
        in_specs=[
            pl.BlockSpec((depth, rows), lambda j: (0, 0)),
            pl.BlockSpec((depth, tile), lambda j: (0, j)),
        ],
        out_specs=pl.BlockSpec((rows, tile), lambda j: (0, j)),
        cost_estimate=pl.CostEstimate(
            flops=2 * rows * depth * width,
            bytes_accessed=2 * rows * depth + 2 * depth * width + 4 * rows * width,
            transcendentals=0,
        ),
    )(left, right)


def stack_kernel(start, width, block, in_ref, out_ref):
    for g in range(out_ref.shape[0]):
        out_ref[g] = in_ref[:, g * block + start:g * block + start + width]


def stack_chunk(amps, groups, start, width):
    sub, total = amps.shape
    block = total // groups
    step = 8
    return pl.pallas_call(
        functools.partial(stack_kernel, start, width, block),
        out_shape=jax.ShapeDtypeStruct((groups, sub, width), amps.dtype),
        grid=(groups // step,),
        in_specs=[pl.BlockSpec((sub, step * block), lambda h: (0, h))],
        out_specs=pl.BlockSpec((step, sub, width), lambda h: (h, 0, 0)),
    )(amps)


def chunk_widths(total):
    first = total * 5 // 8
    return [first, total - first]


def swap_perm(nz, nc):
    return [(z * nc + c, c * nz + z) for z in range(nz) for c in range(nc)]


def local(amps, cycle_int, tile_mask, coulomb, occ_irrep, vir_irrep, occ_energy, vir_energy):
    block_size = BLK
    occupied = occ_energy.shape[0]
    row_blocks = vir_energy.shape[0] // block_size - 1
    kc_rows, jb_all = cycle_int.shape
    rows_here, cols_here = coulomb.shape
    nz = lax.axis_size(Z)
    ny = lax.axis_size(Y)
    ncol = lax.axis_size(COL)
    z = lax.axis_index(Z)
    y = lax.axis_index(Y)
    c = lax.axis_index(COL)
    sub = amps.shape[0]
    span = sub * ny

    ci_rows = lax.dynamic_slice_in_dim(cycle_int, z * span, span, axis=0)
    mask_rows = jnp.repeat(tile_mask.astype(jnp.bfloat16), block_size, axis=0)
    mask_rows = lax.dynamic_slice_in_dim(mask_rows, z * span, span, axis=0)
    masked = (
        ci_rows.reshape(span, jb_all // block_size, block_size) * mask_rows[:, :, None]
    ).reshape(span, jb_all)
    masked_all = lax.all_gather(masked, COL, axis=0, tiled=True)

    groups = lax.axis_size((X, C, Y))
    block = amps.shape[1] // groups
    perm = swap_perm(nz, ncol)
    coulomb_here = lax.ppermute(coulomb, (Z, X, C), perm)
    sums = []
    start = 0
    for k, width in enumerate(chunk_widths(block)):
        piece = stack_chunk(amps, groups, start, width)
        start += width
        if k == 1:
            coulomb_here, piece = lax.optimization_barrier((coulomb_here, piece))
        plane_amps = lax.all_to_all(piece, (X, C, Y), split_axis=0, concat_axis=0, tiled=True)
        partial_value = product(plane_amps.reshape(groups * sub, width), masked_all)
        sums.append(lax.psum_scatter(partial_value, Z, scatter_dimension=1, tiled=True))
    cycle_sum = jnp.concatenate(sums, axis=0)

    row_block = c * ny + y
    row_pos = row_block * rows_here + jnp.arange(rows_here, dtype=jnp.int32)
    col_pos = z * cols_here + jnp.arange(cols_here, dtype=jnp.int32)
    occ_row = row_pos // block_size % occupied
    vir_row = block_size * (row_pos // (occupied * block_size)) + row_pos % block_size
    occ_col = col_pos // block_size % occupied
    vir_col = col_pos % block_size + row_blocks * block_size
    sym_row = jnp.bitwise_xor(lookup(occ_row, occ_irrep), lookup(vir_row, vir_irrep))
    sym_col = jnp.bitwise_xor(lookup(occ_col, occ_irrep), lookup(vir_col, vir_irrep))
    allowed = sym_row[:, None] == sym_col[None, :]
    gap_row = lookup(vir_row, vir_energy) - lookup(occ_row, occ_energy)
    gap_col = lookup(vir_col, vir_energy) - lookup(occ_col, occ_energy)
    denominator = gap_row[:, None] + gap_col[None, :]
    updated = (coulomb_here.astype(jnp.float32) + cycle_sum) / denominator
    out = jnp.where(allowed, updated, jnp.float32(0.0)).astype(jnp.bfloat16)
    return lax.ppermute(out, (Z, X, C), perm)


def solution(mesh):
    nrow, ncol = mesh.devices.shape
    ncore = 2
    nx = ncol // ncore
    nz = ncol
    ny = nrow // nz
    torus = Mesh(mesh.devices.reshape(nz, ny, nx, ncore), (Z, Y, X, C))
    return jax.shard_map(
        local,
        mesh=torus,
        in_specs=(
            P(COL + ROW, None),
            P(COL, None),
            P(COL, None),
            P(ROW, COL),
            P(),
            P(),
            P(),
            P(),
        ),
        out_specs=P(ROW, COL),
        check_vma=False,
    )
```

```python
import functools

import jax
import jax.numpy as jnp
from jax import lax
from jax.experimental import pallas as pl
from jax.experimental.pallas import tpu as pltpu
from jax.sharding import Mesh, PartitionSpec as P

BLK = 64

Z, Y, X, C = "z", "y", "x", "core"
COL = (X, C)
ROW = (Z, Y)


def lookup(positions, values_table):
    entries = jnp.arange(values_table.shape[0], dtype=jnp.int32)
    picked = jnp.where(
        positions[:, None] == entries[None, :],
        values_table[None, :],
        jnp.zeros((), values_table.dtype),
    )
    return jnp.sum(picked, axis=1)


def product_kernel(left_ref, right_ref, out_ref):
    out_ref[...] = lax.dot_general(
        left_ref[...], right_ref[...], (((0,), (0,)), ((), ())), preferred_element_type=jnp.float32
    )


def product(left, right):
    depth, rows = left.shape
    width = right.shape[1]
    tile = 256
    return pl.pallas_call(
        product_kernel,
        out_shape=jax.ShapeDtypeStruct((rows, width), jnp.float32),
        grid=(width // tile,),
        in_specs=[
            pl.BlockSpec((depth, rows), lambda j: (0, 0)),
            pl.BlockSpec((depth, tile), lambda j: (0, j)),
        ],
        out_specs=pl.BlockSpec((rows, tile), lambda j: (0, j)),
        cost_estimate=pl.CostEstimate(
            flops=2 * rows * depth * width,
            bytes_accessed=2 * rows * depth + 2 * depth * width + 4 * rows * width,
            transcendentals=0,
        ),
    )(left, right)


def stack_kernel(start, width, block, in_ref, out_ref):
    for g in range(out_ref.shape[0]):
        out_ref[g] = in_ref[:, g * block + start:g * block + start + width]


def stack_chunk(amps, groups, start, width):
    sub, total = amps.shape
    block = total // groups
    step = 8
    return pl.pallas_call(
        functools.partial(stack_kernel, start, width, block),
        out_shape=jax.ShapeDtypeStruct((groups, sub, width), amps.dtype),
        grid=(groups // step,),
        in_specs=[pl.BlockSpec((sub, step * block), lambda h: (0, h))],
        out_specs=pl.BlockSpec((step, sub, width), lambda h: (h, 0, 0)),
    )(amps)


def chunk_widths(total):
    first = total * 5 // 8
    return [first, total - first]


def swap_perm(nz, nc):
    return [(z * nc + c, c * nz + z) for z in range(nz) for c in range(nc)]


def local(amps, cycle_int, tile_mask, coulomb, occ_irrep, vir_irrep, occ_energy, vir_energy):
    block_size = BLK
    occupied = occ_energy.shape[0]
    row_blocks = vir_energy.shape[0] // block_size - 1
    kc_rows, jb_all = cycle_int.shape
    rows_here, cols_here = coulomb.shape
    nz = lax.axis_size(Z)
    ny = lax.axis_size(Y)
    ncol = lax.axis_size(COL)
    z = lax.axis_index(Z)
    y = lax.axis_index(Y)
    c = lax.axis_index(COL)
    sub = amps.shape[0]
    span = sub * ny

    ci_rows = lax.dynamic_slice_in_dim(cycle_int, z * span, span, axis=0)
    mask_rows = jnp.repeat(tile_mask.astype(jnp.bfloat16), block_size, axis=0)
    mask_rows = lax.dynamic_slice_in_dim(mask_rows, z * span, span, axis=0)
    masked = (
        ci_rows.reshape(span, jb_all // block_size, block_size) * mask_rows[:, :, None]
    ).reshape(span, jb_all)
    masked_all = lax.all_gather(masked, COL, axis=0, tiled=True)

    groups = lax.axis_size((X, C, Y))
    block = amps.shape[1] // groups
    sums = []
    start = 0
    for k, width in enumerate(chunk_widths(block)):
        piece = stack_chunk(amps, groups, start, width)
        start += width
        plane_amps = lax.all_to_all(piece, (X, C, Y), split_axis=0, concat_axis=0, tiled=True)
        partial_value = product(plane_amps.reshape(groups * sub, width), masked_all)
        sums.append(lax.psum_scatter(partial_value, Z, scatter_dimension=1, tiled=True))
    cycle_sum = lax.ppermute(jnp.concatenate(sums, axis=0), (Z, X, C), swap_perm(nz, ncol))

    row_pos = lax.axis_index(ROW) * rows_here + jnp.arange(rows_here, dtype=jnp.int32)
    col_pos = c * cols_here + jnp.arange(cols_here, dtype=jnp.int32)
    occ_row = row_pos // block_size % occupied
    vir_row = block_size * (row_pos // (occupied * block_size)) + row_pos % block_size
    occ_col = col_pos // block_size % occupied
    vir_col = col_pos % block_size + row_blocks * block_size
    sym_row = jnp.bitwise_xor(lookup(occ_row, occ_irrep), lookup(vir_row, vir_irrep))
    sym_col = jnp.bitwise_xor(lookup(occ_col, occ_irrep), lookup(vir_col, vir_irrep))
    allowed = sym_row[:, None] == sym_col[None, :]
    gap_row = lookup(vir_row, vir_energy) - lookup(occ_row, occ_energy)
    gap_col = lookup(vir_col, vir_energy) - lookup(occ_col, occ_energy)
    denominator = gap_row[:, None] + gap_col[None, :]
    updated = (coulomb.astype(jnp.float32) + cycle_sum) / denominator
    out = jnp.where(allowed, updated, jnp.float32(0.0)).astype(jnp.bfloat16)
    return out


def solution(mesh):
    nrow, ncol = mesh.devices.shape
    ncore = 2
    nx = ncol // ncore
    nz = ncol
    ny = nrow // nz
    torus = Mesh(mesh.devices.reshape(nz, ny, nx, ncore), (Z, Y, X, C))
    return jax.shard_map(
        local,
        mesh=torus,
        in_specs=(
            P(COL + ROW, None),
            P(COL, None),
            P(COL, None),
            P(ROW, COL),
            P(),
            P(),
            P(),
            P(),
        ),
        out_specs=P(ROW, COL),
        check_vma=False,
    )
```

```python
import functools

import jax
import jax.numpy as jnp
from jax import lax
from jax.experimental import pallas as pl
from jax.experimental.pallas import tpu as pltpu
from jax.sharding import Mesh, PartitionSpec as P

BLK = 64

Z, Y, X, C = "z", "y", "x", "core"
COL = (X, C)
ROW = (Z, Y)


def lookup(positions, values_table):
    entries = jnp.arange(values_table.shape[0], dtype=jnp.int32)
    picked = jnp.where(
        positions[:, None] == entries[None, :],
        values_table[None, :],
        jnp.zeros((), values_table.dtype),
    )
    return jnp.sum(picked, axis=1)


def product_kernel(left_ref, right_ref, out_ref):
    out_ref[...] = lax.dot_general(
        left_ref[...], right_ref[...], (((0,), (0,)), ((), ())), preferred_element_type=jnp.float32
    )


def product(left, right):
    depth, rows = left.shape
    width = right.shape[1]
    tile = 512
    return pl.pallas_call(
        product_kernel,
        out_shape=jax.ShapeDtypeStruct((rows, width), jnp.float32),
        grid=(width // tile,),
        in_specs=[
            pl.BlockSpec((depth, rows), lambda j: (0, 0)),
            pl.BlockSpec((depth, tile), lambda j: (0, j)),
        ],
        out_specs=pl.BlockSpec((rows, tile), lambda j: (0, j)),
        cost_estimate=pl.CostEstimate(
            flops=2 * rows * depth * width,
            bytes_accessed=2 * rows * depth + 2 * depth * width + 4 * rows * width,
            transcendentals=0,
        ),
    )(left, right)


def stack_kernel(start, width, block, in_ref, out_ref):
    for g in range(out_ref.shape[0]):
        out_ref[g] = in_ref[:, g * block + start:g * block + start + width]


def stack_chunk(amps, groups, start, width):
    sub, total = amps.shape
    block = total // groups
    step = 8
    return pl.pallas_call(
        functools.partial(stack_kernel, start, width, block),
        out_shape=jax.ShapeDtypeStruct((groups, sub, width), amps.dtype),
        grid=(groups // step,),
        in_specs=[pl.BlockSpec((sub, step * block), lambda h: (0, h))],
        out_specs=pl.BlockSpec((step, sub, width), lambda h: (h, 0, 0)),
    )(amps)


def chunk_widths(total):
    first = total * 5 // 8
    return [first, total - first]


def swap_perm(nz, nc):
    return [(z * nc + c, c * nz + z) for z in range(nz) for c in range(nc)]


def local(amps, cycle_int, tile_mask, coulomb, occ_irrep, vir_irrep, occ_energy, vir_energy):
    block_size = BLK
    occupied = occ_energy.shape[0]
    row_blocks = vir_energy.shape[0] // block_size - 1
    kc_rows, jb_all = cycle_int.shape
    rows_here, cols_here = coulomb.shape
    nz = lax.axis_size(Z)
    ny = lax.axis_size(Y)
    ncol = lax.axis_size(COL)
    z = lax.axis_index(Z)
    y = lax.axis_index(Y)
    c = lax.axis_index(COL)
    sub = amps.shape[0]
    span = sub * ny

    ci_rows = lax.dynamic_slice_in_dim(cycle_int, z * span, span, axis=0)
    mask_rows = jnp.repeat(tile_mask.astype(jnp.bfloat16), block_size, axis=0)
    mask_rows = lax.dynamic_slice_in_dim(mask_rows, z * span, span, axis=0)
    masked = (
        ci_rows.reshape(span, jb_all // block_size, block_size) * mask_rows[:, :, None]
    ).reshape(span, jb_all)
    masked_all = lax.all_gather(masked, COL, axis=0, tiled=True)

    groups = lax.axis_size((X, C, Y))
    block = amps.shape[1] // groups
    perm = swap_perm(nz, ncol)
    coulomb_here = lax.ppermute(coulomb, (Z, X, C), perm)
    sums = []
    start = 0
    for k, width in enumerate(chunk_widths(block)):
        piece = stack_chunk(amps, groups, start, width)
        start += width
        if k == 1:
            coulomb_here, piece = lax.optimization_barrier((coulomb_here, piece))
        plane_amps = lax.all_to_all(piece, (X, C, Y), split_axis=0, concat_axis=0, tiled=True)
        partial_value = product(plane_amps.reshape(groups * sub, width), masked_all)
        sums.append(lax.psum_scatter(partial_value, Z, scatter_dimension=1, tiled=True))
    cycle_sum = jnp.concatenate(sums, axis=0)

    row_block = c * ny + y
    row_pos = row_block * rows_here + jnp.arange(rows_here, dtype=jnp.int32)
    col_pos = z * cols_here + jnp.arange(cols_here, dtype=jnp.int32)
    occ_row = row_pos // block_size % occupied
    vir_row = block_size * (row_pos // (occupied * block_size)) + row_pos % block_size
    occ_col = col_pos // block_size % occupied
    vir_col = col_pos % block_size + row_blocks * block_size
    sym_row = jnp.bitwise_xor(lookup(occ_row, occ_irrep), lookup(vir_row, vir_irrep))
    sym_col = jnp.bitwise_xor(lookup(occ_col, occ_irrep), lookup(vir_col, vir_irrep))
    allowed = sym_row[:, None] == sym_col[None, :]
    gap_row = lookup(vir_row, vir_energy) - lookup(occ_row, occ_energy)
    gap_col = lookup(vir_col, vir_energy) - lookup(occ_col, occ_energy)
    denominator = gap_row[:, None] + gap_col[None, :]
    updated = (coulomb_here.astype(jnp.float32) + cycle_sum) / denominator
    out = jnp.where(allowed, updated, jnp.float32(0.0)).astype(jnp.bfloat16)
    return lax.ppermute(out, (Z, X, C), perm)


def solution(mesh):
    nrow, ncol = mesh.devices.shape
    ncore = 2
    nx = ncol // ncore
    nz = ncol
    ny = nrow // nz
    torus = Mesh(mesh.devices.reshape(nz, ny, nx, ncore), (Z, Y, X, C))
    return jax.shard_map(
        local,
        mesh=torus,
        in_specs=(
            P(COL + ROW, None),
            P(COL, None),
            P(COL, None),
            P(ROW, COL),
            P(),
            P(),
            P(),
            P(),
        ),
        out_specs=P(ROW, COL),
        check_vma=False,
    )
```

```python
import functools

import jax
import jax.numpy as jnp
from jax import lax
from jax.experimental import pallas as pl
from jax.experimental.pallas import tpu as pltpu
from jax.sharding import Mesh, PartitionSpec as P

BLK = 64

Z, Y, X, C = "z", "y", "x", "core"
COL = (X, C)
ROW = (Z, Y)


def lookup(positions, values_table):
    entries = jnp.arange(values_table.shape[0], dtype=jnp.int32)
    picked = jnp.where(
        positions[:, None] == entries[None, :],
        values_table[None, :],
        jnp.zeros((), values_table.dtype),
    )
    return jnp.sum(picked, axis=1)


def product_kernel(left_ref, right_ref, out_ref):
    out_ref[...] = lax.dot_general(
        left_ref[...], right_ref[...], (((0,), (0,)), ((), ())), preferred_element_type=jnp.float32
    )


def product(left, right):
    depth, rows = left.shape
    width = right.shape[1]
    tile = 1024
    return pl.pallas_call(
        product_kernel,
        out_shape=jax.ShapeDtypeStruct((rows, width), jnp.float32),
        grid=(width // tile,),
        in_specs=[
            pl.BlockSpec((depth, rows), lambda j: (0, 0)),
            pl.BlockSpec((depth, tile), lambda j: (0, j)),
        ],
        out_specs=pl.BlockSpec((rows, tile), lambda j: (0, j)),
        cost_estimate=pl.CostEstimate(
            flops=2 * rows * depth * width,
            bytes_accessed=2 * rows * depth + 2 * depth * width + 4 * rows * width,
            transcendentals=0,
        ),
    )(left, right)


def stack_kernel(start, width, block, in_ref, out_ref):
    for g in range(out_ref.shape[0]):
        out_ref[g] = in_ref[:, g * block + start:g * block + start + width]


def stack_chunk(amps, groups, start, width):
    sub, total = amps.shape
    block = total // groups
    step = 8
    return pl.pallas_call(
        functools.partial(stack_kernel, start, width, block),
        out_shape=jax.ShapeDtypeStruct((groups, sub, width), amps.dtype),
        grid=(groups // step,),
        in_specs=[pl.BlockSpec((sub, step * block), lambda h: (0, h))],
        out_specs=pl.BlockSpec((step, sub, width), lambda h: (h, 0, 0)),
    )(amps)


def chunk_widths(total):
    first = total * 5 // 8
    return [first, total - first]


def swap_perm(nz, nc):
    return [(z * nc + c, c * nz + z) for z in range(nz) for c in range(nc)]


def local(amps, cycle_int, tile_mask, coulomb, occ_irrep, vir_irrep, occ_energy, vir_energy):
    block_size = BLK
    occupied = occ_energy.shape[0]
    row_blocks = vir_energy.shape[0] // block_size - 1
    kc_rows, jb_all = cycle_int.shape
    rows_here, cols_here = coulomb.shape
    nz = lax.axis_size(Z)
    ny = lax.axis_size(Y)
    ncol = lax.axis_size(COL)
    z = lax.axis_index(Z)
    y = lax.axis_index(Y)
    c = lax.axis_index(COL)
    sub = amps.shape[0]
    span = sub * ny

    ci_rows = lax.dynamic_slice_in_dim(cycle_int, z * span, span, axis=0)
    mask_rows = jnp.repeat(tile_mask.astype(jnp.bfloat16), block_size, axis=0)
    mask_rows = lax.dynamic_slice_in_dim(mask_rows, z * span, span, axis=0)
    masked = (
        ci_rows.reshape(span, jb_all // block_size, block_size) * mask_rows[:, :, None]
    ).reshape(span, jb_all)
    masked_all = lax.all_gather(masked, COL, axis=0, tiled=True)

    groups = lax.axis_size((X, C, Y))
    block = amps.shape[1] // groups
    perm = swap_perm(nz, ncol)
    coulomb_here = lax.ppermute(coulomb, (Z, X, C), perm)
    sums = []
    start = 0
    for k, width in enumerate(chunk_widths(block)):
        piece = stack_chunk(amps, groups, start, width)
        start += width
        if k == 1:
            coulomb_here, piece = lax.optimization_barrier((coulomb_here, piece))
        plane_amps = lax.all_to_all(piece, (X, C, Y), split_axis=0, concat_axis=0, tiled=True)
        partial_value = product(plane_amps.reshape(groups * sub, width), masked_all)
        sums.append(lax.psum_scatter(partial_value, Z, scatter_dimension=1, tiled=True))
    cycle_sum = jnp.concatenate(sums, axis=0)

    row_block = c * ny + y
    row_pos = row_block * rows_here + jnp.arange(rows_here, dtype=jnp.int32)
    col_pos = z * cols_here + jnp.arange(cols_here, dtype=jnp.int32)
    occ_row = row_pos // block_size % occupied
    vir_row = block_size * (row_pos // (occupied * block_size)) + row_pos % block_size
    occ_col = col_pos // block_size % occupied
    vir_col = col_pos % block_size + row_blocks * block_size
    sym_row = jnp.bitwise_xor(lookup(occ_row, occ_irrep), lookup(vir_row, vir_irrep))
    sym_col = jnp.bitwise_xor(lookup(occ_col, occ_irrep), lookup(vir_col, vir_irrep))
    allowed = sym_row[:, None] == sym_col[None, :]
    gap_row = lookup(vir_row, vir_energy) - lookup(occ_row, occ_energy)
    gap_col = lookup(vir_col, vir_energy) - lookup(occ_col, occ_energy)
    denominator = gap_row[:, None] + gap_col[None, :]
    updated = (coulomb_here.astype(jnp.float32) + cycle_sum) / denominator
    out = jnp.where(allowed, updated, jnp.float32(0.0)).astype(jnp.bfloat16)
    return lax.ppermute(out, (Z, X, C), perm)


def solution(mesh):
    nrow, ncol = mesh.devices.shape
    ncore = 2
    nx = ncol // ncore
    nz = ncol
    ny = nrow // nz
    torus = Mesh(mesh.devices.reshape(nz, ny, nx, ncore), (Z, Y, X, C))
    return jax.shard_map(
        local,
        mesh=torus,
        in_specs=(
            P(COL + ROW, None),
            P(COL, None),
            P(COL, None),
            P(ROW, COL),
            P(),
            P(),
            P(),
            P(),
        ),
        out_specs=P(ROW, COL),
        check_vma=False,
    )
```

```python
import functools

import jax
import jax.numpy as jnp
from jax import lax
from jax.experimental import pallas as pl
from jax.experimental.pallas import tpu as pltpu
from jax.sharding import Mesh, PartitionSpec as P

BLK = 64

Z, Y, X, C = "z", "y", "x", "core"
COL = (X, C)
ROW = (Z, Y)


def lookup(positions, values_table):
    entries = jnp.arange(values_table.shape[0], dtype=jnp.int32)
    picked = jnp.where(
        positions[:, None] == entries[None, :],
        values_table[None, :],
        jnp.zeros((), values_table.dtype),
    )
    return jnp.sum(picked, axis=1)


def product_kernel(left_ref, right_ref, out_ref):
    out_ref[...] = lax.dot_general(
        left_ref[...], right_ref[...], (((0,), (0,)), ((), ())), preferred_element_type=jnp.float32
    )


def product(left, right):
    depth, rows = left.shape
    width = right.shape[1]
    tile = 512
    return pl.pallas_call(
        product_kernel,
        out_shape=jax.ShapeDtypeStruct((rows, width), jnp.float32),
        grid=(width // tile,),
        in_specs=[
            pl.BlockSpec((depth, rows), lambda j: (0, 0)),
            pl.BlockSpec((depth, tile), lambda j: (0, j)),
        ],
        out_specs=pl.BlockSpec((rows, tile), lambda j: (0, j)),
        cost_estimate=pl.CostEstimate(
            flops=2 * rows * depth * width,
            bytes_accessed=2 * rows * depth + 2 * depth * width + 4 * rows * width,
            transcendentals=0,
        ),
    )(left, right)


def stack_kernel(start, width, block, in_ref, out_ref):
    for g in range(out_ref.shape[0]):
        out_ref[g] = in_ref[:, g * block + start:g * block + start + width]


def stack_chunk(amps, groups, start, width):
    sub, total = amps.shape
    block = total // groups
    step = 8
    return pl.pallas_call(
        functools.partial(stack_kernel, start, width, block),
        out_shape=jax.ShapeDtypeStruct((groups, sub, width), amps.dtype),
        grid=(groups // step,),
        in_specs=[pl.BlockSpec((sub, step * block), lambda h: (0, h))],
        out_specs=pl.BlockSpec((step, sub, width), lambda h: (h, 0, 0)),
    )(amps)


def chunk_widths(total):
    first = total * 7 // 12
    return [first, total - first]


def swap_perm(nz, nc):
    return [(z * nc + c, c * nz + z) for z in range(nz) for c in range(nc)]


def local(amps, cycle_int, tile_mask, coulomb, occ_irrep, vir_irrep, occ_energy, vir_energy):
    block_size = BLK
    occupied = occ_energy.shape[0]
    row_blocks = vir_energy.shape[0] // block_size - 1
    kc_rows, jb_all = cycle_int.shape
    rows_here, cols_here = coulomb.shape
    nz = lax.axis_size(Z)
    ny = lax.axis_size(Y)
    ncol = lax.axis_size(COL)
    z = lax.axis_index(Z)
    y = lax.axis_index(Y)
    c = lax.axis_index(COL)
    sub = amps.shape[0]
    span = sub * ny

    ci_rows = lax.dynamic_slice_in_dim(cycle_int, z * span, span, axis=0)
    mask_rows = jnp.repeat(tile_mask.astype(jnp.bfloat16), block_size, axis=0)
    mask_rows = lax.dynamic_slice_in_dim(mask_rows, z * span, span, axis=0)
    masked = (
        ci_rows.reshape(span, jb_all // block_size, block_size) * mask_rows[:, :, None]
    ).reshape(span, jb_all)
    masked_all = lax.all_gather(masked, COL, axis=0, tiled=True)

    groups = lax.axis_size((X, C, Y))
    block = amps.shape[1] // groups
    perm = swap_perm(nz, ncol)
    coulomb_here = lax.ppermute(coulomb, (Z, X, C), perm)
    sums = []
    start = 0
    for k, width in enumerate(chunk_widths(block)):
        piece = stack_chunk(amps, groups, start, width)
        start += width
        if k == 1:
            coulomb_here, piece = lax.optimization_barrier((coulomb_here, piece))
        plane_amps = lax.all_to_all(piece, (X, C, Y), split_axis=0, concat_axis=0, tiled=True)
        partial_value = product(plane_amps.reshape(groups * sub, width), masked_all)
        sums.append(lax.psum_scatter(partial_value, Z, scatter_dimension=1, tiled=True))
    cycle_sum = jnp.concatenate(sums, axis=0)

    row_block = c * ny + y
    row_pos = row_block * rows_here + jnp.arange(rows_here, dtype=jnp.int32)
    col_pos = z * cols_here + jnp.arange(cols_here, dtype=jnp.int32)
    occ_row = row_pos // block_size % occupied
    vir_row = block_size * (row_pos // (occupied * block_size)) + row_pos % block_size
    occ_col = col_pos // block_size % occupied
    vir_col = col_pos % block_size + row_blocks * block_size
    sym_row = jnp.bitwise_xor(lookup(occ_row, occ_irrep), lookup(vir_row, vir_irrep))
    sym_col = jnp.bitwise_xor(lookup(occ_col, occ_irrep), lookup(vir_col, vir_irrep))
    allowed = sym_row[:, None] == sym_col[None, :]
    gap_row = lookup(vir_row, vir_energy) - lookup(occ_row, occ_energy)
    gap_col = lookup(vir_col, vir_energy) - lookup(occ_col, occ_energy)
    denominator = gap_row[:, None] + gap_col[None, :]
    updated = (coulomb_here.astype(jnp.float32) + cycle_sum) / denominator
    out = jnp.where(allowed, updated, jnp.float32(0.0)).astype(jnp.bfloat16)
    return lax.ppermute(out, (Z, X, C), perm)


def solution(mesh):
    nrow, ncol = mesh.devices.shape
    ncore = 2
    nx = ncol // ncore
    nz = ncol
    ny = nrow // nz
    torus = Mesh(mesh.devices.reshape(nz, ny, nx, ncore), (Z, Y, X, C))
    return jax.shard_map(
        local,
        mesh=torus,
        in_specs=(
            P(COL + ROW, None),
            P(COL, None),
            P(COL, None),
            P(ROW, COL),
            P(),
            P(),
            P(),
            P(),
        ),
        out_specs=P(ROW, COL),
        check_vma=False,
    )
```
